256 devices in a mesh: row: 8 (over y, core), col: 32 (over x, z).
Axes of the slice: x: 4, y: 4, z: 8, core: 2. Of those that a mesh axis runs over, the one named last changes fastest.
Arguments:
- inputs: bfloat16 [1024, 8192], P('row', 'col'), may hold values from -6 to 6
- out_grad: bfloat16 [1024, 8192], P('row', 'col'), may hold values from -6 to 6
- in_weight: bfloat16 [8192, 3, 8192], P('col', None, 'row'), may hold values from -0.0625 to 0.0625
- out_weight: bfloat16 [8192, 8192], P('row', 'col'), may hold values from -0.0625 to 0.0625
- filter_taps: float32 [8192, 7], P('row'), may hold values from -2.4 to 2.4
Outputs:
- result: bfloat16 [1024, 8192], P('row', 'col')
- input_grad: bfloat16 [1024, 8192], P('row', 'col')
- in_grad: bfloat16 [8192, 3, 8192], P('col', None, 'row')
- out_w_grad: bfloat16 [8192, 8192], P('row', 'col')
- filter_grad: float32 [8192, 7], P(('row', 'col'))
The draws below stay inside these ranges and needn't reach their ends.
All inputs are finite; a program needn't handle non-finite values.
Results may differ from the reference program's by a relative error of at most 0.03.
Values may be sent and summed in bfloat16 or wider, within the bound.
No kernel may reach another device: no remote copies, remote signals or barrier semaphores. Data moves between devices by JAX's collectives and lax.ppermute only.
A program may use at most 64 MiB of HBM per device.

```python
import math
import jax
import jax.numpy as jnp
from jax import lax

D = 8192
KSIZE = 7
TOKENS = 1024
N_COL = 32


def levels(stream_key, extent, cuts, least, top_value):
    level, own = 1.0, jax.random.fold_in(stream_key, 6)
    for dim, parts in cuts:
        steps = jnp.exp(jax.random.uniform(jax.random.fold_in(own, dim), (parts,), jnp.float32, least / len(cuts), top_value / len(cuts)))
        level = level * jnp.repeat(steps, extent[dim] // parts).reshape([-1 if axis == dim else 1 for axis in range(len(extent))])
    return level


def normal_values(own_key, shape, spread, most, shards=(), kind=jnp.bfloat16):
    loudness = levels(own_key, shape, shards, -0.22, 0.18) if shards else 1.0
    array = jax.random.normal(own_key, shape, jnp.float32) * spread * loudness
    return jnp.minimum(jnp.maximum(array, -most), most).astype(kind)


def setup_inputs(seed: int = 0) -> dict:
    streams_of = jax.random.split(jax.random.key(seed), 6)
    return {
        "inputs": normal_values(streams_of[0], (TOKENS, D), 1.0, 6.0, ((0, 8), (1, 32))),
        "out_grad": normal_values(streams_of[1], (TOKENS, D), 1.0, 6.0, ((0, 8), (1, 32))),
        "in_weight": normal_values(streams_of[2], (D, 3, D), D ** -0.5, 0.0625, ((0, 32), (2, 8))),
        "out_weight": normal_values(streams_of[3], (D, D), D ** -0.5, 0.0625, ((0, 8), (1, 32))),
        "filter_taps": normal_values(streams_of[4], (D, KSIZE), 0.4, 2.4, ((0, 8),), jnp.float32),
    }


def round_keep(value):
    rounded = lax.optimization_barrier(value.astype(jnp.bfloat16))
    return rounded.astype(jnp.float32)

def reference(inputs, out_grad, in_weight, out_weight, filter_taps):
    col_width = D // N_COL
    conv_lag = KSIZE - 1
    grad_scale = 1.0 / math.sqrt(TOKENS)
    block_ids = jnp.arange(N_COL, dtype=jnp.int32)

    def in_block(accum, block_id):
        begin = (block_id * col_width).astype(jnp.int32)
        source = lax.dynamic_slice_in_dim(inputs, begin, col_width, 1)
        weights = lax.dynamic_slice_in_dim(in_weight, begin, col_width, 0).reshape(col_width, 3 * D)
        partial_sum = jnp.dot(source, weights, preferred_element_type=jnp.float32)
        return (accum + round_keep(partial_sum), None)
    summed, _ = lax.scan(in_block, jnp.zeros((TOKENS, 3 * D), jnp.float32), block_ids)
    mixed_qkv = summed.astype(jnp.bfloat16).reshape(TOKENS, 3, D)
    query_part = mixed_qkv[:, 0].astype(jnp.float32)
    key_part = mixed_qkv[:, 1].astype(jnp.float32)
    value_part = mixed_qkv[:, 2].astype(jnp.float32)
    kv_product = key_part * value_part
    padded = jnp.concatenate([jnp.zeros((conv_lag, D), jnp.float32), kv_product], 0)
    conv_out = jnp.zeros((TOKENS, D), jnp.float32)
    for offset in range(KSIZE):
        conv_out = conv_out + filter_taps[:, offset] * padded[conv_lag - offset:conv_lag - offset + TOKENS]
    gated_out = (query_part * conv_out).astype(jnp.bfloat16)
    projected = jnp.dot(gated_out, out_weight, preferred_element_type=jnp.float32)
    result = (inputs.astype(jnp.float32) + projected).astype(jnp.bfloat16)
    out_w_grad = (lax.dot_general(gated_out, out_grad, (((0,), (0,)), ((), ())), preferred_element_type=jnp.float32) * grad_scale).astype(jnp.bfloat16)

    def grad_block(accum, block_id):
        begin = (block_id * col_width).astype(jnp.int32)
        cotangent = lax.dynamic_slice_in_dim(out_grad, begin, col_width, 1)
        weights = lax.dynamic_slice_in_dim(out_weight, begin, col_width, 1)
        partial_sum = lax.dot_general(cotangent, weights, (((1,), (1,)), ((), ())), preferred_element_type=jnp.float32)
        return (accum + round_keep(partial_sum), None)
    grad_gated, _ = lax.scan(grad_block, jnp.zeros((TOKENS, D), jnp.float32), block_ids)
    grad_query = grad_gated * conv_out
    grad_conv = grad_gated * query_part
    padded_back = jnp.concatenate([grad_conv, jnp.zeros((conv_lag, D), jnp.float32)], 0)
    grad_product = jnp.zeros((TOKENS, D), jnp.float32)
    tap_terms = []
    for offset in range(KSIZE):
        grad_product = grad_product + filter_taps[:, offset] * padded_back[offset:offset + TOKENS]
        tap_terms.append(lax.optimization_barrier(jnp.sum(grad_conv * padded[conv_lag - offset:conv_lag - offset + TOKENS], axis=0)))
    filter_grad = jnp.stack(tap_terms, axis=1) * grad_scale
    grad_mixed = jnp.stack([grad_query, grad_product * value_part, grad_product * key_part], axis=1).astype(jnp.bfloat16)
    grad_flat = grad_mixed.reshape(TOKENS, 3 * D)
    in_grad = (lax.dot_general(inputs, grad_flat, (((0,), (0,)), ((), ())), preferred_element_type=jnp.float32) * grad_scale).astype(jnp.bfloat16).reshape(D, 3, D)
    back_sum = lax.dot_general(grad_flat, in_weight.reshape(D, 3 * D), (((1,), (1,)), ((), ())), preferred_element_type=jnp.float32)
    input_grad = (out_grad.astype(jnp.float32) + back_sum).astype(jnp.bfloat16)
    return (result, input_grad, in_grad, out_w_grad, filter_grad)
```

```python
import math

import jax
import jax.numpy as jnp
from jax import lax
from jax.sharding import PartitionSpec as P


def rows_in(operand):
    return lax.all_gather(operand, "row", axis=0, tiled=True)


def fold_rows(summand):
    return lax.psum_scatter(
        summand.astype(jnp.bfloat16), "row", scatter_dimension=0, tiled=True
    ).astype(jnp.float32)


def sum_cols(summand):
    return lax.psum(summand.astype(jnp.bfloat16), "col")


def shifted(values, by):
    tokens = values.shape[0]
    if by == 0:
        return values
    pad = jnp.zeros((abs(by),) + values.shape[1:], values.dtype)
    if by > 0:
        return jnp.concatenate([pad, values[: tokens - by]], 0)
    return jnp.concatenate([values[-by:], pad], 0)


def on_device(inputs, out_grad, in_weight, out_weight, filter_taps):
    col_width = inputs.shape[1]
    row_width = out_weight.shape[0]
    kernel_len = filter_taps.shape[1]
    weight_flat = in_weight.reshape(col_width, 3 * row_width)
    whole_in = rows_in(inputs)
    all_tokens = whole_in.shape[0]
    grad_scale = 1.0 / math.sqrt(all_tokens)

    in_term = jnp.dot(whole_in, weight_flat, preferred_element_type=jnp.float32)
    mixed_qkv = sum_cols(in_term).reshape(all_tokens, 3, row_width)
    query_part = mixed_qkv[:, 0].astype(jnp.float32)
    key_part = mixed_qkv[:, 1].astype(jnp.float32)
    value_part = mixed_qkv[:, 2].astype(jnp.float32)
    kv_product = key_part * value_part
    conv_out = jnp.zeros_like(kv_product)
    for offset in range(kernel_len):
        conv_out = conv_out + filter_taps[:, offset] * shifted(kv_product, offset)
    gated_all = (query_part * conv_out).astype(jnp.bfloat16)

    projected = fold_rows(
        jnp.dot(gated_all, out_weight, preferred_element_type=jnp.float32)
    )
    result = (inputs.astype(jnp.float32) + projected).astype(jnp.bfloat16)

    whole_grad = rows_in(out_grad)
    out_w_grad = (
        lax.dot_general(
            gated_all, whole_grad, (((0,), (0,)), ((), ())), preferred_element_type=jnp.float32
        )
        * grad_scale
    ).astype(jnp.bfloat16)
    dy_term = lax.dot_general(
        whole_grad, out_weight, (((1,), (1,)), ((), ())), preferred_element_type=jnp.float32
    )
    grad_gated = sum_cols(dy_term).astype(jnp.float32)
    grad_query = grad_gated * conv_out
    grad_conv = grad_gated * query_part
    grad_product = jnp.zeros_like(grad_conv)
    tap_terms = []
    for offset in range(kernel_len):
        grad_product = grad_product + filter_taps[:, offset] * shifted(grad_conv, -offset)
        tap_terms.append(jnp.sum(grad_conv * shifted(kv_product, offset), axis=0))
    tap_stack = jnp.stack(tap_terms, axis=1)
    cols = lax.axis_size("col")
    own = row_width // cols
    filter_grad = (
        lax.dynamic_slice_in_dim(tap_stack, lax.axis_index("col") * own, own, 0) * grad_scale
    )
    grad_mixed = jnp.stack(
        [grad_query, grad_product * value_part, grad_product * key_part], axis=1
    ).astype(jnp.bfloat16)
    grad_flat = grad_mixed.reshape(all_tokens, 3 * row_width)
    in_grad = (
        (
            lax.dot_general(
                whole_in, grad_flat, (((0,), (0,)), ((), ())), preferred_element_type=jnp.float32
            )
            * grad_scale
        )
        .astype(jnp.bfloat16)
        .reshape(col_width, 3, row_width)
    )
    back_sum = fold_rows(
        lax.dot_general(
            grad_flat, weight_flat, (((1,), (1,)), ((), ())), preferred_element_type=jnp.float32
        )
    )
    input_grad = (out_grad.astype(jnp.float32) + back_sum).astype(jnp.bfloat16)
    return (result, input_grad, in_grad, out_w_grad, filter_grad)


def solution(mesh):
    placed = (
        P("row", "col"),
        P("row", "col"),
        P("col", None, "row"),
        P("row", "col"),
        P("row", None),
    )
    return jax.shard_map(
        on_device,
        mesh=mesh,
        in_specs=placed,
        out_specs=(
            P("row", "col"),
            P("row", "col"),
            P("col", None, "row"),
            P("row", "col"),
            P(("row", "col"), None),
        ),
        check_vma=False,
    )
```

```python
import math

import jax
import jax.numpy as jnp
from jax import lax
from jax.experimental import pallas as pl
from jax.experimental.pallas import tpu as pltpu
from jax.sharding import PartitionSpec as P


def rows_in(operand):
    return lax.all_gather(operand, "row", axis=0, tiled=True)


def fold_rows(summand):
    return lax.psum_scatter(
        summand.astype(jnp.bfloat16), "row", scatter_dimension=0, tiled=True
    ).astype(jnp.float32)


def sum_cols(summand):
    return lax.psum(summand.astype(jnp.bfloat16), "col")


def gate_body(q_ref, k_ref, v_ref, g_ref, t_ref, gated_ref, gq_ref, gk_ref, gv_ref, ts_ref):
    tokens, width = q_ref.shape
    kernel_len = t_ref.shape[0]
    q = q_ref[...].astype(jnp.float32)
    k = k_ref[...].astype(jnp.float32)
    v = v_ref[...].astype(jnp.float32)
    g = g_ref[...].astype(jnp.float32)
    taps = t_ref[...]
    row = lax.broadcasted_iota(jnp.int32, (tokens, width), 0)
    kv = k * v
    kv_lag = [kv]
    for i in range(1, kernel_len):
        kv_lag.append(jnp.where(row >= i, pltpu.roll(kv, i, 0), 0.0))
    conv = jnp.zeros_like(kv)
    for i in range(kernel_len):
        conv = conv + taps[i : i + 1, :] * kv_lag[i]
    gated_ref[...] = (q * conv).astype(gated_ref.dtype)
    gc = g * q
    gp = jnp.zeros_like(gc)
    sums = []
    for i in range(kernel_len):
        if i == 0:
            lead = gc
        else:
            lead = jnp.where(row < tokens - i, pltpu.roll(gc, tokens - i, 0), 0.0)
        gp = gp + taps[i : i + 1, :] * lead
        sums.append(jnp.sum(gc * kv_lag[i], axis=0, keepdims=True))
    sums.append(jnp.zeros((ts_ref.shape[0] - kernel_len, width), jnp.float32))
    ts_ref[...] = jnp.concatenate(sums, 0)
    gq_ref[...] = (g * conv).astype(gq_ref.dtype)
    gk_ref[...] = (gp * v).astype(gk_ref.dtype)
    gv_ref[...] = (gp * k).astype(gv_ref.dtype)


def gate_kernel(mixed_flat, grad_gated, taps_t, width=128):
    tokens, three_ch = mixed_flat.shape
    channels = three_ch // 3
    kernel_len = taps_t.shape[0]
    tiles = channels // width
    col = lambda off: pl.BlockSpec((tokens, width), lambda j: (0, j + off))
    half = jax.ShapeDtypeStruct((tokens, channels), jnp.bfloat16)
    return pl.pallas_call(
        gate_body,
        grid=(tiles,),
        in_specs=[
            col(0),
            col(tiles),
            col(2 * tiles),
            col(0),
            pl.BlockSpec((kernel_len, width), lambda j: (0, j)),
        ],
        out_specs=[col(0), col(0), col(0), col(0), pl.BlockSpec((8, width), lambda j: (0, j))],
        out_shape=[half, half, half, half, jax.ShapeDtypeStruct((8, channels), jnp.float32)],
        cost_estimate=pl.CostEstimate(
            flops=60 * tokens * channels, transcendentals=0, bytes_accessed=18 * tokens * channels
        ),
    )(mixed_flat, mixed_flat, mixed_flat, grad_gated, taps_t)


def on_device(inputs, out_grad, in_weight, out_weight, filter_taps):
    col_width = inputs.shape[1]
    row_width = out_weight.shape[0]
    weight_flat = in_weight.reshape(col_width, 3 * row_width)
    whole_in = rows_in(inputs)
    all_tokens = whole_in.shape[0]
    grad_scale = 1.0 / math.sqrt(all_tokens)

    in_term = jnp.dot(whole_in, weight_flat, preferred_element_type=jnp.float32)
    whole_grad = rows_in(out_grad)
    dy_term = lax.dot_general(
        whole_grad, out_weight, (((1,), (1,)), ((), ())), preferred_element_type=jnp.float32
    )
    mixed_flat = sum_cols(in_term)
    grad_gated = sum_cols(dy_term)
    gated_all, grad_query, grad_key, grad_value, tap_sums = gate_kernel(
        mixed_flat, grad_gated, filter_taps.T
    )

    projected = fold_rows(
        jnp.dot(gated_all, out_weight, preferred_element_type=jnp.float32)
    )
    result = (inputs.astype(jnp.float32) + projected).astype(jnp.bfloat16)
    out_w_grad = (
        lax.dot_general(
            gated_all, whole_grad, (((0,), (0,)), ((), ())), preferred_element_type=jnp.float32
        )
        * grad_scale
    ).astype(jnp.bfloat16)
    cols = lax.axis_size("col")
    own = row_width // cols
    kernel_len = filter_taps.shape[1]
    filter_grad = (
        lax.dynamic_slice_in_dim(tap_sums[:kernel_len], lax.axis_index("col") * own, own, 1).T
        * grad_scale
    )
    grad_flat = jnp.concatenate([grad_query, grad_key, grad_value], axis=1)
    in_grad = (
        (
            lax.dot_general(
                whole_in, grad_flat, (((0,), (0,)), ((), ())), preferred_element_type=jnp.float32
            )
            * grad_scale
        )
        .astype(jnp.bfloat16)
        .reshape(col_width, 3, row_width)
    )
    back_sum = fold_rows(
        lax.dot_general(
            grad_flat, weight_flat, (((1,), (1,)), ((), ())), preferred_element_type=jnp.float32
        )
    )
    input_grad = (out_grad.astype(jnp.float32) + back_sum).astype(jnp.bfloat16)
    return (result, input_grad, in_grad, out_w_grad, filter_grad)


def solution(mesh):
    placed = (
        P("row", "col"),
        P("row", "col"),
        P("col", None, "row"),
        P("row", "col"),
        P("row", None),
    )
    return jax.shard_map(
        on_device,
        mesh=mesh,
        in_specs=placed,
        out_specs=(
            P("row", "col"),
            P("row", "col"),
            P("col", None, "row"),
            P("row", "col"),
            P(("row", "col"), None),
        ),
        check_vma=False,
    )
```

```python
import math

import jax
import jax.numpy as jnp
from jax import lax
from jax.experimental import pallas as pl
from jax.experimental.pallas import tpu as pltpu
from jax.sharding import PartitionSpec as P


def rows_in(operand):
    return lax.all_gather(operand, "row", axis=0, tiled=True)


def fold_rows(summand):
    return lax.psum_scatter(
        summand.astype(jnp.bfloat16), "row", scatter_dimension=0, tiled=True
    ).astype(jnp.float32)


def sum_cols(summand):
    return lax.psum(summand.astype(jnp.bfloat16), "col")


def gate_body(q_ref, k_ref, v_ref, g_ref, t_ref, gated_ref, gq_ref, gk_ref, gv_ref, ts_ref):
    tokens, width = q_ref.shape
    kernel_len = t_ref.shape[0]
    q = q_ref[...].astype(jnp.float32)
    k = k_ref[...].astype(jnp.float32)
    v = v_ref[...].astype(jnp.float32)
    g = g_ref[...].astype(jnp.float32)
    taps = t_ref[...]
    row = lax.broadcasted_iota(jnp.int32, (tokens, width), 0)
    kv = k * v
    kv_lag = [kv]
    for i in range(1, kernel_len):
        kv_lag.append(jnp.where(row >= i, pltpu.roll(kv, i, 0), 0.0))
    conv = jnp.zeros_like(kv)
    for i in range(kernel_len):
        conv = conv + taps[i : i + 1, :] * kv_lag[i]
    gated_ref[...] = (q * conv).astype(gated_ref.dtype)
    gc = g * q
    gp = jnp.zeros_like(gc)
    sums = []
    for i in range(kernel_len):
        if i == 0:
            lead = gc
        else:
            lead = jnp.where(row < tokens - i, pltpu.roll(gc, tokens - i, 0), 0.0)
        gp = gp + taps[i : i + 1, :] * lead
        sums.append(jnp.sum(gc * kv_lag[i], axis=0, keepdims=True))
    sums.append(jnp.zeros((ts_ref.shape[0] - kernel_len, width), jnp.float32))
    ts_ref[...] = jnp.concatenate(sums, 0)
    gq_ref[...] = (g * conv).astype(gq_ref.dtype)
    gk_ref[...] = (gp * v).astype(gk_ref.dtype)
    gv_ref[...] = (gp * k).astype(gv_ref.dtype)


def gate_kernel(mixed_flat, grad_gated, taps_t, width=128):
    tokens, three_ch = mixed_flat.shape
    channels = three_ch // 3
    kernel_len = taps_t.shape[0]
    tiles = channels // width
    col = lambda off: pl.BlockSpec((tokens, width), lambda j: (0, j + off))
    half = jax.ShapeDtypeStruct((tokens, channels), jnp.bfloat16)
    return pl.pallas_call(
        gate_body,
        grid=(tiles,),
        in_specs=[
            col(0),
            col(tiles),
            col(2 * tiles),
            col(0),
            pl.BlockSpec((kernel_len, width), lambda j: (0, j)),
        ],
        out_specs=[col(0), col(0), col(0), col(0), pl.BlockSpec((8, width), lambda j: (0, j))],
        out_shape=[half, half, half, half, jax.ShapeDtypeStruct((8, channels), jnp.float32)],
        cost_estimate=pl.CostEstimate(
            flops=60 * tokens * channels, transcendentals=0, bytes_accessed=18 * tokens * channels
        ),
    )(mixed_flat, mixed_flat, mixed_flat, grad_gated, taps_t)


def on_device(inputs, out_grad, in_weight, out_weight, filter_taps):
    col_width = inputs.shape[1]
    row_width = out_weight.shape[0]
    weight_flat = in_weight.reshape(col_width, 3 * row_width)
    both_in = rows_in(jnp.concatenate([inputs, out_grad], axis=1))
    whole_in = both_in[:, :col_width]
    whole_grad = both_in[:, col_width:]
    all_tokens = whole_in.shape[0]
    grad_scale = 1.0 / math.sqrt(all_tokens)

    in_term = jnp.dot(whole_in, weight_flat, preferred_element_type=jnp.float32)
    dy_term = lax.dot_general(
        whole_grad, out_weight, (((1,), (1,)), ((), ())), preferred_element_type=jnp.float32
    )
    mixed_flat = sum_cols(in_term)
    grad_gated = sum_cols(dy_term)
    gated_all, grad_query, grad_key, grad_value, tap_sums = gate_kernel(
        mixed_flat, grad_gated, filter_taps.T
    )

    projected_term = jnp.dot(gated_all, out_weight, preferred_element_type=jnp.float32)
    out_w_grad = (
        lax.dot_general(
            gated_all, whole_grad, (((0,), (0,)), ((), ())), preferred_element_type=jnp.float32
        )
        * grad_scale
    ).astype(jnp.bfloat16)
    cols = lax.axis_size("col")
    own = row_width // cols
    kernel_len = filter_taps.shape[1]
    filter_grad = (
        lax.dynamic_slice_in_dim(tap_sums[:kernel_len], lax.axis_index("col") * own, own, 1).T
        * grad_scale
    )
    grad_flat = jnp.concatenate([grad_query, grad_key, grad_value], axis=1)
    in_grad = (
        (
            lax.dot_general(
                whole_in, grad_flat, (((0,), (0,)), ((), ())), preferred_element_type=jnp.float32
            )
            * grad_scale
        )
        .astype(jnp.bfloat16)
        .reshape(col_width, 3, row_width)
    )
    back_term = lax.dot_general(
        grad_flat, weight_flat, (((1,), (1,)), ((), ())), preferred_element_type=jnp.float32
    )
    both_sums = fold_rows(jnp.concatenate([projected_term, back_term], axis=1))
    projected = both_sums[:, :col_width]
    back_sum = both_sums[:, col_width:]
    result = (inputs.astype(jnp.float32) + projected).astype(jnp.bfloat16)
    input_grad = (out_grad.astype(jnp.float32) + back_sum).astype(jnp.bfloat16)
    return (result, input_grad, in_grad, out_w_grad, filter_grad)


def solution(mesh):
    placed = (
        P("row", "col"),
        P("row", "col"),
        P("col", None, "row"),
        P("row", "col"),
        P("row", None),
    )
    return jax.shard_map(
        on_device,
        mesh=mesh,
        in_specs=placed,
        out_specs=(
            P("row", "col"),
            P("row", "col"),
            P("col", None, "row"),
            P("row", "col"),
            P(("row", "col"), None),
        ),
        check_vma=False,
    )
```

```python
import math

import jax
import jax.numpy as jnp
from jax import lax
from jax.experimental import pallas as pl
from jax.experimental.pallas import tpu as pltpu
from jax.sharding import PartitionSpec as P


def rows_in(operand):
    devices = lax.axis_size("row")
    me = lax.axis_index("row")
    arrived = [operand]
    for dist in range(1, devices):
        pairs = [(i, (i + dist) % devices) for i in range(devices)]
        arrived.append(lax.ppermute(operand, "row", pairs))
    stacked = jnp.stack(arrived)
    order = (me - jnp.arange(devices)) % devices
    return stacked[order].reshape((devices * operand.shape[0],) + operand.shape[1:])


def fold_rows(summand):
    return lax.psum_scatter(
        summand.astype(jnp.bfloat16), "row", scatter_dimension=0, tiled=True
    ).astype(jnp.float32)


def sum_cols(summand):
    return lax.psum(summand.astype(jnp.bfloat16), "col")


def gate_body(q_ref, k_ref, v_ref, g_ref, t_ref, gated_ref, gq_ref, gk_ref, gv_ref, ts_ref):
    tokens, width = q_ref.shape
    kernel_len = t_ref.shape[0]
    q = q_ref[...].astype(jnp.float32)
    k = k_ref[...].astype(jnp.float32)
    v = v_ref[...].astype(jnp.float32)
    g = g_ref[...].astype(jnp.float32)
    taps = t_ref[...]
    row = lax.broadcasted_iota(jnp.int32, (tokens, width), 0)
    kv = k * v
    kv_lag = [kv]
    for i in range(1, kernel_len):
        kv_lag.append(jnp.where(row >= i, pltpu.roll(kv, i, 0), 0.0))
    conv = jnp.zeros_like(kv)
    for i in range(kernel_len):
        conv = conv + taps[i : i + 1, :] * kv_lag[i]
    gated_ref[...] = (q * conv).astype(gated_ref.dtype)
    gc = g * q
    gp = jnp.zeros_like(gc)
    sums = []
    for i in range(kernel_len):
        if i == 0:
            lead = gc
        else:
            lead = jnp.where(row < tokens - i, pltpu.roll(gc, tokens - i, 0), 0.0)
        gp = gp + taps[i : i + 1, :] * lead
        sums.append(jnp.sum(gc * kv_lag[i], axis=0, keepdims=True))
    sums.append(jnp.zeros((ts_ref.shape[0] - kernel_len, width), jnp.float32))
    ts_ref[...] = jnp.concatenate(sums, 0)
    gq_ref[...] = (g * conv).astype(gq_ref.dtype)
    gk_ref[...] = (gp * v).astype(gk_ref.dtype)
    gv_ref[...] = (gp * k).astype(gv_ref.dtype)


def gate_kernel(mixed_flat, grad_gated, taps_t, width=128):
    tokens, three_ch = mixed_flat.shape
    channels = three_ch // 3
    kernel_len = taps_t.shape[0]
    tiles = channels // width
    col = lambda off: pl.BlockSpec((tokens, width), lambda j: (0, j + off))
    half = jax.ShapeDtypeStruct((tokens, channels), jnp.bfloat16)
    return pl.pallas_call(
        gate_body,
        grid=(tiles,),
        in_specs=[
            col(0),
            col(tiles),
            col(2 * tiles),
            col(0),
            pl.BlockSpec((kernel_len, width), lambda j: (0, j)),
        ],
        out_specs=[col(0), col(0), col(0), col(0), pl.BlockSpec((8, width), lambda j: (0, j))],
        out_shape=[half, half, half, half, jax.ShapeDtypeStruct((8, channels), jnp.float32)],
        cost_estimate=pl.CostEstimate(
            flops=60 * tokens * channels, transcendentals=0, bytes_accessed=18 * tokens * channels
        ),
    )(mixed_flat, mixed_flat, mixed_flat, grad_gated, taps_t)


def on_device(inputs, out_grad, in_weight, out_weight, filter_taps):
    col_width = inputs.shape[1]
    row_width = out_weight.shape[0]
    weight_flat = in_weight.reshape(col_width, 3 * row_width)
    both_in = rows_in(jnp.concatenate([inputs, out_grad], axis=1))
    whole_in = both_in[:, :col_width]
    whole_grad = both_in[:, col_width:]
    all_tokens = whole_in.shape[0]
    grad_scale = 1.0 / math.sqrt(all_tokens)

    in_term = jnp.dot(whole_in, weight_flat, preferred_element_type=jnp.float32)
    dy_term = lax.dot_general(
        whole_grad, out_weight, (((1,), (1,)), ((), ())), preferred_element_type=jnp.float32
    )
    mixed_flat = sum_cols(in_term)
    grad_gated = sum_cols(dy_term)
    gated_all, grad_query, grad_key, grad_value, tap_sums = gate_kernel(
        mixed_flat, grad_gated, filter_taps.T
    )

    projected_term = jnp.dot(gated_all, out_weight, preferred_element_type=jnp.float32)
    out_w_grad = (
        lax.dot_general(
            gated_all, whole_grad, (((0,), (0,)), ((), ())), preferred_element_type=jnp.float32
        )
        * grad_scale
    ).astype(jnp.bfloat16)
    cols = lax.axis_size("col")
    own = row_width // cols
    kernel_len = filter_taps.shape[1]
    filter_grad = (
        lax.dynamic_slice_in_dim(tap_sums[:kernel_len], lax.axis_index("col") * own, own, 1).T
        * grad_scale
    )
    grad_flat = jnp.concatenate([grad_query, grad_key, grad_value], axis=1)
    in_grad = (
        (
            lax.dot_general(
                whole_in, grad_flat, (((0,), (0,)), ((), ())), preferred_element_type=jnp.float32
            )
            * grad_scale
        )
        .astype(jnp.bfloat16)
        .reshape(col_width, 3, row_width)
    )
    back_term = lax.dot_general(
        grad_flat, weight_flat, (((1,), (1,)), ((), ())), preferred_element_type=jnp.float32
    )
    both_sums = fold_rows(jnp.concatenate([projected_term, back_term], axis=1))
    projected = both_sums[:, :col_width]
    back_sum = both_sums[:, col_width:]
    result = (inputs.astype(jnp.float32) + projected).astype(jnp.bfloat16)
    input_grad = (out_grad.astype(jnp.float32) + back_sum).astype(jnp.bfloat16)
    return (result, input_grad, in_grad, out_w_grad, filter_grad)


def solution(mesh):
    placed = (
        P("row", "col"),
        P("row", "col"),
        P("col", None, "row"),
        P("row", "col"),
        P("row", None),
    )
    return jax.shard_map(
        on_device,
        mesh=mesh,
        in_specs=placed,
        out_specs=(
            P("row", "col"),
            P("row", "col"),
            P("col", None, "row"),
            P("row", "col"),
            P(("row", "col"), None),
        ),
        check_vma=False,
    )
```

```python
import math

import jax
import jax.numpy as jnp
from jax import lax
from jax.experimental import pallas as pl
from jax.experimental.pallas import tpu as pltpu
from jax.sharding import PartitionSpec as P


def rows_in(operand):
    return lax.all_gather(operand, "row", axis=0, tiled=True)


def fold_rows(summand):
    return lax.psum_scatter(
        summand.astype(jnp.bfloat16), "row", scatter_dimension=0, tiled=True
    ).astype(jnp.float32)


def sum_cols(summand):
    return lax.psum(summand.astype(jnp.bfloat16), "col")


def gate_body(q_ref, k_ref, v_ref, g_ref, t_ref, gated_ref, gq_ref, gk_ref, gv_ref, ts_ref):
    tokens, width = q_ref.shape
    kernel_len = t_ref.shape[0]
    q = q_ref[...].astype(jnp.float32)
    k = k_ref[...].astype(jnp.float32)
    v = v_ref[...].astype(jnp.float32)
    g = g_ref[...].astype(jnp.float32)
    taps = t_ref[...]
    edge = lax.broadcasted_iota(jnp.int32, (8, width), 0)

    def lagged(x, i):
        rolled = pltpu.roll(x, i, 0)
        return jnp.concatenate([jnp.where(edge >= i, rolled[:8], 0.0), rolled[8:]], 0)

    def leading(x, i):
        rolled = pltpu.roll(x, tokens - i, 0)
        return jnp.concatenate([rolled[:-8], jnp.where(edge < 8 - i, rolled[-8:], 0.0)], 0)

    kv = k * v
    kv_lag = [kv] + [lagged(kv, i) for i in range(1, kernel_len)]
    conv = taps[0:1, :] * kv_lag[0]
    for i in range(1, kernel_len):
        conv = conv + taps[i : i + 1, :] * kv_lag[i]
    gated_ref[...] = (q * conv).astype(gated_ref.dtype)
    gc = g * q
    gp = taps[0:1, :] * gc
    sums = []
    for i in range(kernel_len):
        if i > 0:
            gp = gp + taps[i : i + 1, :] * leading(gc, i)
        sums.append(jnp.sum(gc * kv_lag[i], axis=0, keepdims=True))
    sums.append(jnp.zeros((ts_ref.shape[0] - kernel_len, width), jnp.float32))
    ts_ref[...] = jnp.concatenate(sums, 0)
    gq_ref[...] = (g * conv).astype(gq_ref.dtype)
    gk_ref[...] = (gp * v).astype(gk_ref.dtype)
    gv_ref[...] = (gp * k).astype(gv_ref.dtype)


def gate_kernel(mixed_flat, grad_gated, taps_t, width=256):
    tokens, three_ch = mixed_flat.shape
    channels = three_ch // 3
    kernel_len = taps_t.shape[0]
    tiles = channels // width
    col = lambda off: pl.BlockSpec((tokens, width), lambda j: (0, j + off))
    half = jax.ShapeDtypeStruct((tokens, channels), jnp.bfloat16)
    return pl.pallas_call(
        gate_body,
        grid=(tiles,),
        in_specs=[
            col(0),
            col(tiles),
            col(2 * tiles),
            col(0),
            pl.BlockSpec((kernel_len, width), lambda j: (0, j)),
        ],
        out_specs=[col(0), col(0), col(0), col(0), pl.BlockSpec((8, width), lambda j: (0, j))],
        out_shape=[half, half, half, half, jax.ShapeDtypeStruct((8, channels), jnp.float32)],
        cost_estimate=pl.CostEstimate(
            flops=60 * tokens * channels, transcendentals=0, bytes_accessed=18 * tokens * channels
        ),
    )(mixed_flat, mixed_flat, mixed_flat, grad_gated, taps_t)


def on_device(inputs, out_grad, in_weight, out_weight, filter_taps):
    col_width = inputs.shape[1]
    row_width = out_weight.shape[0]
    weight_flat = in_weight.reshape(col_width, 3 * row_width)
    both_in = rows_in(jnp.concatenate([inputs, out_grad], axis=1))
    whole_in = both_in[:, :col_width]
    whole_grad = both_in[:, col_width:]
    all_tokens = whole_in.shape[0]
    grad_scale = 1.0 / math.sqrt(all_tokens)

    in_term = jnp.dot(whole_in, weight_flat, preferred_element_type=jnp.float32)
    dy_term = lax.dot_general(
        whole_grad, out_weight, (((1,), (1,)), ((), ())), preferred_element_type=jnp.float32
    )
    mixed_flat = sum_cols(in_term)
    grad_gated = sum_cols(dy_term)
    gated_all, grad_query, grad_key, grad_value, tap_sums = gate_kernel(
        mixed_flat, grad_gated, filter_taps.T
    )

    projected_term = jnp.dot(gated_all, out_weight, preferred_element_type=jnp.float32)
    out_w_grad = (
        lax.dot_general(
            gated_all, whole_grad, (((0,), (0,)), ((), ())), preferred_element_type=jnp.float32
        )
        * grad_scale
    ).astype(jnp.bfloat16)
    cols = lax.axis_size("col")
    own = row_width // cols
    kernel_len = filter_taps.shape[1]
    filter_grad = (
        lax.dynamic_slice_in_dim(tap_sums[:kernel_len], lax.axis_index("col") * own, own, 1).T
        * grad_scale
    )
    grad_flat = jnp.concatenate([grad_query, grad_key, grad_value], axis=1)
    in_grad = (
        (
            lax.dot_general(
                whole_in, grad_flat, (((0,), (0,)), ((), ())), preferred_element_type=jnp.float32
            )
            * grad_scale
        )
        .astype(jnp.bfloat16)
        .reshape(col_width, 3, row_width)
    )
    back_term = lax.dot_general(
        grad_flat, weight_flat, (((1,), (1,)), ((), ())), preferred_element_type=jnp.float32
    )
    both_sums = fold_rows(jnp.concatenate([projected_term, back_term], axis=1))
    projected = both_sums[:, :col_width]
    back_sum = both_sums[:, col_width:]
    result = (inputs.astype(jnp.float32) + projected).astype(jnp.bfloat16)
    input_grad = (out_grad.astype(jnp.float32) + back_sum).astype(jnp.bfloat16)
    return (result, input_grad, in_grad, out_w_grad, filter_grad)


def solution(mesh):
    placed = (
        P("row", "col"),
        P("row", "col"),
        P("col", None, "row"),
        P("row", "col"),
        P("row", None),
    )
    return jax.shard_map(
        on_device,
        mesh=mesh,
        in_specs=placed,
        out_specs=(
            P("row", "col"),
            P("row", "col"),
            P("col", None, "row"),
            P("row", "col"),
            P(("row", "col"), None),
        ),
        check_vma=False,
    )
```

```python
import math

import jax
import jax.numpy as jnp
from jax import lax
from jax.experimental import pallas as pl
from jax.experimental.pallas import tpu as pltpu
from jax.sharding import PartitionSpec as P


def rows_in(operand):
    return lax.all_gather(operand, "row", axis=1, tiled=True)


def fold_rows(summand):
    return lax.psum_scatter(
        summand.astype(jnp.bfloat16), "row", scatter_dimension=1, tiled=True
    ).astype(jnp.float32)


def sum_cols(summand):
    return lax.psum(summand.astype(jnp.bfloat16), "col")


def gate_body(q_ref, k_ref, v_ref, g_ref, t_ref, gated_ref, gq_ref, gk_ref, gv_ref, ts_ref):
    tokens, width = q_ref.shape
    kernel_len = t_ref.shape[0]
    q = q_ref[...].astype(jnp.float32)
    k = k_ref[...].astype(jnp.float32)
    v = v_ref[...].astype(jnp.float32)
    g = g_ref[...].astype(jnp.float32)
    taps = t_ref[...]
    row = lax.broadcasted_iota(jnp.int32, (tokens, width), 0)
    kv = k * v
    kv_lag = [kv]
    for i in range(1, kernel_len):
        kv_lag.append(jnp.where(row >= i, pltpu.roll(kv, i, 0), 0.0))
    conv = taps[0:1, :] * kv_lag[0]
    for i in range(1, kernel_len):
        conv = conv + taps[i : i + 1, :] * kv_lag[i]
    gated_ref[...] = (q * conv).astype(gated_ref.dtype)
    gc = g * q
    gp = taps[0:1, :] * gc
    sums = []
    for i in range(kernel_len):
        if i > 0:
            lead = jnp.where(row < tokens - i, pltpu.roll(gc, tokens - i, 0), 0.0)
            gp = gp + taps[i : i + 1, :] * lead
        sums.append(jnp.sum(gc * kv_lag[i], axis=0, keepdims=True))
    sums.append(jnp.zeros((ts_ref.shape[0] - kernel_len, width), jnp.float32))
    ts_ref[...] = jnp.concatenate(sums, 0)
    gq_ref[...] = (g * conv).astype(gq_ref.dtype)
    gk_ref[...] = (gp * v).astype(gk_ref.dtype)
    gv_ref[...] = (gp * k).astype(gv_ref.dtype)


def gate_kernel(mixed_flat, grad_gated, taps_t, width=128):
    tokens, three_ch = mixed_flat.shape
    channels = three_ch // 3
    kernel_len = taps_t.shape[0]
    tiles = channels // width
    col = lambda off: pl.BlockSpec((tokens, width), lambda j: (0, j + off))
    half = jax.ShapeDtypeStruct((tokens, channels), jnp.bfloat16)
    return pl.pallas_call(
        gate_body,
        grid=(tiles,),
        in_specs=[
            col(0),
            col(tiles),
            col(2 * tiles),
            col(0),
            pl.BlockSpec((kernel_len, width), lambda j: (0, j)),
        ],
        out_specs=[col(0), col(0), col(0), col(0), pl.BlockSpec((8, width), lambda j: (0, j))],
        out_shape=[half, half, half, half, jax.ShapeDtypeStruct((8, channels), jnp.float32)],
        cost_estimate=pl.CostEstimate(
            flops=60 * tokens * channels, transcendentals=0, bytes_accessed=18 * tokens * channels
        ),
    )(mixed_flat, mixed_flat, mixed_flat, grad_gated, taps_t)


def on_device(inputs, out_grad, in_weight, out_weight, filter_taps):
    col_width = inputs.shape[1]
    row_width = out_weight.shape[0]
    weight_flat = in_weight.reshape(col_width, 3 * row_width)
    both_in = rows_in(jnp.stack([inputs, out_grad]))
    whole_in = both_in[0]
    whole_grad = both_in[1]
    all_tokens = whole_in.shape[0]
    grad_scale = 1.0 / math.sqrt(all_tokens)

    in_term = jnp.dot(whole_in, weight_flat, preferred_element_type=jnp.float32)
    dy_term = lax.dot_general(
        whole_grad, out_weight, (((1,), (1,)), ((), ())), preferred_element_type=jnp.float32
    )
    mixed_flat = sum_cols(in_term)
    grad_gated = sum_cols(dy_term)
    gated_all, grad_query, grad_key, grad_value, tap_sums = gate_kernel(
        mixed_flat, grad_gated, filter_taps.T
    )

    projected_term = jnp.dot(gated_all, out_weight, preferred_element_type=jnp.float32)
    out_w_grad = (
        lax.dot_general(
            gated_all, whole_grad, (((0,), (0,)), ((), ())), preferred_element_type=jnp.float32
        )
        * grad_scale
    ).astype(jnp.bfloat16)
    cols = lax.axis_size("col")
    own = row_width // cols
    kernel_len = filter_taps.shape[1]
    filter_grad = (
        lax.dynamic_slice_in_dim(tap_sums[:kernel_len], lax.axis_index("col") * own, own, 1).T
        * grad_scale
    )
    grad_flat = jnp.concatenate([grad_query, grad_key, grad_value], axis=1)
    in_grad = (
        (
            lax.dot_general(
                whole_in, grad_flat, (((0,), (0,)), ((), ())), preferred_element_type=jnp.float32
            )
            * grad_scale
        )
        .astype(jnp.bfloat16)
        .reshape(col_width, 3, row_width)
    )
    back_term = lax.dot_general(
        grad_flat, weight_flat, (((1,), (1,)), ((), ())), preferred_element_type=jnp.float32
    )
    both_sums = fold_rows(jnp.stack([projected_term, back_term]))
    projected = both_sums[0]
    back_sum = both_sums[1]
    result = (inputs.astype(jnp.float32) + projected).astype(jnp.bfloat16)
    input_grad = (out_grad.astype(jnp.float32) + back_sum).astype(jnp.bfloat16)
    return (result, input_grad, in_grad, out_w_grad, filter_grad)


def solution(mesh):
    placed = (
        P("row", "col"),
        P("row", "col"),
        P("col", None, "row"),
        P("row", "col"),
        P("row", None),
    )
    return jax.shard_map(
        on_device,
        mesh=mesh,
        in_specs=placed,
        out_specs=(
            P("row", "col"),
            P("row", "col"),
            P("col", None, "row"),
            P("row", "col"),
            P(("row", "col"), None),
        ),
        check_vma=False,
    )
```

```python
import math

import jax
import jax.numpy as jnp
from jax import lax
from jax.experimental import pallas as pl
from jax.experimental.pallas import tpu as pltpu
from jax.sharding import PartitionSpec as P


def rows_in(operand):
    return lax.all_gather(operand, "row", axis=1, tiled=True)


def fold_rows(summand):
    return lax.psum_scatter(
        summand.astype(jnp.bfloat16), "row", scatter_dimension=1, tiled=True
    ).astype(jnp.float32)


def sum_cols(summand):
    return lax.psum(summand.astype(jnp.bfloat16), "col")


def gate_body(q_ref, k_ref, v_ref, g_ref, t_ref, gated_ref, gq_ref, gk_ref, gv_ref):
    tokens, width = q_ref.shape
    kernel_len = t_ref.shape[0]
    q = q_ref[...].astype(jnp.float32)
    k = k_ref[...].astype(jnp.float32)
    v = v_ref[...].astype(jnp.float32)
    g = g_ref[...].astype(jnp.float32)
    taps = t_ref[...]
    row = lax.broadcasted_iota(jnp.int32, (tokens, width), 0)
    kv = k * v
    conv = taps[0:1, :] * kv
    for i in range(1, kernel_len):
        conv = conv + taps[i : i + 1, :] * jnp.where(row >= i, pltpu.roll(kv, i, 0), 0.0)
    gated_ref[...] = (q * conv).astype(gated_ref.dtype)
    gc = g * q
    gp = taps[0:1, :] * gc
    for i in range(1, kernel_len):
        lead = jnp.where(row < tokens - i, pltpu.roll(gc, tokens - i, 0), 0.0)
        gp = gp + taps[i : i + 1, :] * lead
    gq_ref[...] = (g * conv).astype(gq_ref.dtype)
    gk_ref[...] = (gp * v).astype(gk_ref.dtype)
    gv_ref[...] = (gp * k).astype(gv_ref.dtype)


def tap_body(q_ref, k_ref, v_ref, g_ref, ts_ref):
    tokens, width = q_ref.shape
    kernel_len = ts_ref.shape[0] - 1
    q = q_ref[...].astype(jnp.float32)
    k = k_ref[...].astype(jnp.float32)
    v = v_ref[...].astype(jnp.float32)
    g = g_ref[...].astype(jnp.float32)
    row = lax.broadcasted_iota(jnp.int32, (tokens, width), 0)
    kv = k * v
    gc = g * q
    sums = [jnp.sum(gc * kv, axis=0, keepdims=True)]
    for i in range(1, kernel_len):
        lagged = jnp.where(row >= i, pltpu.roll(kv, i, 0), 0.0)
        sums.append(jnp.sum(gc * lagged, axis=0, keepdims=True))
    sums.append(jnp.zeros((ts_ref.shape[0] - kernel_len, width), jnp.float32))
    ts_ref[...] = jnp.concatenate(sums, 0)


def gate_kernel(mixed_flat, grad_gated, taps_t, width=128):
    tokens, three_ch = mixed_flat.shape
    channels = three_ch // 3
    kernel_len = taps_t.shape[0]
    tiles = channels // width
    col = lambda off: pl.BlockSpec((tokens, width), lambda j: (0, j + off))
    half = jax.ShapeDtypeStruct((tokens, channels), jnp.bfloat16)
    operands = (mixed_flat, mixed_flat, mixed_flat, grad_gated)
    gated, grad_query, grad_key, grad_value = pl.pallas_call(
        gate_body,
        grid=(tiles,),
        in_specs=[
            col(0),
            col(tiles),
            col(2 * tiles),
            col(0),
            pl.BlockSpec((kernel_len, width), lambda j: (0, j)),
        ],
        out_specs=[col(0), col(0), col(0), col(0)],
        out_shape=[half, half, half, half],
        cost_estimate=pl.CostEstimate(
            flops=45 * tokens * channels, transcendentals=0, bytes_accessed=16 * tokens * channels
        ),
    )(*operands, taps_t)
    tap_sums = pl.pallas_call(
        tap_body,
        grid=(tiles,),
        in_specs=[col(0), col(tiles), col(2 * tiles), col(0)],
        out_specs=pl.BlockSpec((kernel_len + 1, width), lambda j: (0, j)),
        out_shape=jax.ShapeDtypeStruct((kernel_len + 1, channels), jnp.float32),
        cost_estimate=pl.CostEstimate(
            flops=30 * tokens * channels, transcendentals=0, bytes_accessed=8 * tokens * channels
        ),
    )(*operands)
    return gated, grad_query, grad_key, grad_value, tap_sums


def on_device(inputs, out_grad, in_weight, out_weight, filter_taps):
    col_width = inputs.shape[1]
    row_width = out_weight.shape[0]
    weight_flat = in_weight.reshape(col_width, 3 * row_width)
    both_in = rows_in(jnp.stack([inputs, out_grad]))
    whole_in = both_in[0]
    whole_grad = both_in[1]
    all_tokens = whole_in.shape[0]
    grad_scale = 1.0 / math.sqrt(all_tokens)

    in_term = jnp.dot(whole_in, weight_flat, preferred_element_type=jnp.float32)
    dy_term = lax.dot_general(
        whole_grad, out_weight, (((1,), (1,)), ((), ())), preferred_element_type=jnp.float32
    )
    mixed_flat = sum_cols(in_term)
    grad_gated = sum_cols(dy_term)
    gated_all, grad_query, grad_key, grad_value, tap_sums = gate_kernel(
        mixed_flat, grad_gated, filter_taps.T
    )

    projected_term = jnp.dot(gated_all, out_weight, preferred_element_type=jnp.float32)
    out_w_grad = (
        lax.dot_general(
            gated_all, whole_grad, (((0,), (0,)), ((), ())), preferred_element_type=jnp.float32
        )
        * grad_scale
    ).astype(jnp.bfloat16)
    cols = lax.axis_size("col")
    own = row_width // cols
    kernel_len = filter_taps.shape[1]
    filter_grad = (
        lax.dynamic_slice_in_dim(tap_sums[:kernel_len], lax.axis_index("col") * own, own, 1).T
        * grad_scale
    )
    grad_flat = jnp.concatenate([grad_query, grad_key, grad_value], axis=1)
    in_grad = (
        (
            lax.dot_general(
                whole_in, grad_flat, (((0,), (0,)), ((), ())), preferred_element_type=jnp.float32
            )
            * grad_scale
        )
        .astype(jnp.bfloat16)
        .reshape(col_width, 3, row_width)
    )
    back_term = lax.dot_general(
        grad_flat, weight_flat, (((1,), (1,)), ((), ())), preferred_element_type=jnp.float32
    )
    both_sums = fold_rows(jnp.stack([projected_term, back_term]))
    projected = both_sums[0]
    back_sum = both_sums[1]
    result = (inputs.astype(jnp.float32) + projected).astype(jnp.bfloat16)
    input_grad = (out_grad.astype(jnp.float32) + back_sum).astype(jnp.bfloat16)
    return (result, input_grad, in_grad, out_w_grad, filter_grad)


def solution(mesh):
    placed = (
        P("row", "col"),
        P("row", "col"),
        P("col", None, "row"),
        P("row", "col"),
        P("row", None),
    )
    return jax.shard_map(
        on_device,
        mesh=mesh,
        in_specs=placed,
        out_specs=(
            P("row", "col"),
            P("row", "col"),
            P("col", None, "row"),
            P("row", "col"),
            P(("row", "col"), None),
        ),
        check_vma=False,
    )
```

```python
import math

import jax
import jax.numpy as jnp
from jax import lax
from jax.experimental import pallas as pl
from jax.experimental.pallas import tpu as pltpu
from jax.sharding import PartitionSpec as P


def rows_in(operand):
    return lax.all_gather(operand, "row", axis=1, tiled=True)


def fold_rows(summand):
    devices = lax.axis_size("row")
    me = lax.axis_index("row")
    lead, rows = summand.shape[0], summand.shape[1] // devices
    parts = summand.astype(jnp.bfloat16).reshape((lead, devices, rows) + summand.shape[2:])
    total = lax.dynamic_index_in_dim(parts, me, 1, keepdims=False).astype(jnp.float32)
    for dist in range(1, devices):
        pairs = [(i, (i + dist) % devices) for i in range(devices)]
        block = lax.dynamic_index_in_dim(parts, (me + dist) % devices, 1, keepdims=False)
        total = total + lax.ppermute(block, "row", pairs).astype(jnp.float32)
    return total


def sum_cols(summand):
    return lax.psum(summand.astype(jnp.bfloat16), "col")


def gate_body(q_ref, k_ref, v_ref, g_ref, t_ref, gated_ref, gq_ref, gk_ref, gv_ref):
    tokens, width = q_ref.shape
    kernel_len = t_ref.shape[0]
    q = q_ref[...].astype(jnp.float32)
    k = k_ref[...].astype(jnp.float32)
    v = v_ref[...].astype(jnp.float32)
    g = g_ref[...].astype(jnp.float32)
    taps = t_ref[...]
    row = lax.broadcasted_iota(jnp.int32, (tokens, width), 0)
    kv = k * v
    conv = taps[0:1, :] * kv
    for i in range(1, kernel_len):
        conv = conv + taps[i : i + 1, :] * jnp.where(row >= i, pltpu.roll(kv, i, 0), 0.0)
    gated_ref[...] = (q * conv).astype(gated_ref.dtype)
    gc = g * q
    gp = taps[0:1, :] * gc
    for i in range(1, kernel_len):
        lead = jnp.where(row < tokens - i, pltpu.roll(gc, tokens - i, 0), 0.0)
        gp = gp + taps[i : i + 1, :] * lead
    gq_ref[...] = (g * conv).astype(gq_ref.dtype)
    gk_ref[...] = (gp * v).astype(gk_ref.dtype)
    gv_ref[...] = (gp * k).astype(gv_ref.dtype)


def tap_body(q_ref, k_ref, v_ref, g_ref, ts_ref):
    tokens, width = q_ref.shape
    kernel_len = ts_ref.shape[0] - 1
    q = q_ref[...].astype(jnp.float32)
    k = k_ref[...].astype(jnp.float32)
    v = v_ref[...].astype(jnp.float32)
    g = g_ref[...].astype(jnp.float32)
    row = lax.broadcasted_iota(jnp.int32, (tokens, width), 0)
    kv = k * v
    gc = g * q
    sums = [jnp.sum(gc * kv, axis=0, keepdims=True)]
    for i in range(1, kernel_len):
        lagged = jnp.where(row >= i, pltpu.roll(kv, i, 0), 0.0)
        sums.append(jnp.sum(gc * lagged, axis=0, keepdims=True))
    sums.append(jnp.zeros((ts_ref.shape[0] - kernel_len, width), jnp.float32))
    ts_ref[...] = jnp.concatenate(sums, 0)


def gate_kernel(mixed_flat, grad_gated, taps_t, width=128):
    tokens, three_ch = mixed_flat.shape
    channels = three_ch // 3
    kernel_len = taps_t.shape[0]
    tiles = channels // width
    col = lambda off: pl.BlockSpec((tokens, width), lambda j: (0, j + off))
    half = jax.ShapeDtypeStruct((tokens, channels), jnp.bfloat16)
    operands = (mixed_flat, mixed_flat, mixed_flat, grad_gated)
    gated, grad_query, grad_key, grad_value = pl.pallas_call(
        gate_body,
        grid=(tiles,),
        in_specs=[
            col(0),
            col(tiles),
            col(2 * tiles),
            col(0),
            pl.BlockSpec((kernel_len, width), lambda j: (0, j)),
        ],
        out_specs=[col(0), col(0), col(0), col(0)],
        out_shape=[half, half, half, half],
        cost_estimate=pl.CostEstimate(
            flops=45 * tokens * channels, transcendentals=0, bytes_accessed=16 * tokens * channels
        ),
    )(*operands, taps_t)
    tap_sums = pl.pallas_call(
        tap_body,
        grid=(tiles,),
        in_specs=[col(0), col(tiles), col(2 * tiles), col(0)],
        out_specs=pl.BlockSpec((kernel_len + 1, width), lambda j: (0, j)),
        out_shape=jax.ShapeDtypeStruct((kernel_len + 1, channels), jnp.float32),
        cost_estimate=pl.CostEstimate(
            flops=30 * tokens * channels, transcendentals=0, bytes_accessed=8 * tokens * channels
        ),
    )(*operands)
    return gated, grad_query, grad_key, grad_value, tap_sums


def on_device(inputs, out_grad, in_weight, out_weight, filter_taps):
    col_width = inputs.shape[1]
    row_width = out_weight.shape[0]
    weight_flat = in_weight.reshape(col_width, 3 * row_width)
    both_in = rows_in(jnp.stack([inputs, out_grad]))
    whole_in = both_in[0]
    whole_grad = both_in[1]
    all_tokens = whole_in.shape[0]
    grad_scale = 1.0 / math.sqrt(all_tokens)

    in_term = jnp.dot(whole_in, weight_flat, preferred_element_type=jnp.float32)
    dy_term = lax.dot_general(
        whole_grad, out_weight, (((1,), (1,)), ((), ())), preferred_element_type=jnp.float32
    )
    mixed_flat = sum_cols(in_term)
    grad_gated = sum_cols(dy_term)
    gated_all, grad_query, grad_key, grad_value, tap_sums = gate_kernel(
        mixed_flat, grad_gated, filter_taps.T
    )

    projected_term = jnp.dot(gated_all, out_weight, preferred_element_type=jnp.float32)
    out_w_grad = (
        lax.dot_general(
            gated_all, whole_grad, (((0,), (0,)), ((), ())), preferred_element_type=jnp.float32
        )
        * grad_scale
    ).astype(jnp.bfloat16)
    cols = lax.axis_size("col")
    own = row_width // cols
    kernel_len = filter_taps.shape[1]
    filter_grad = (
        lax.dynamic_slice_in_dim(tap_sums[:kernel_len], lax.axis_index("col") * own, own, 1).T
        * grad_scale
    )
    grad_flat = jnp.concatenate([grad_query, grad_key, grad_value], axis=1)
    in_grad = (
        (
            lax.dot_general(
                whole_in, grad_flat, (((0,), (0,)), ((), ())), preferred_element_type=jnp.float32
            )
            * grad_scale
        )
        .astype(jnp.bfloat16)
        .reshape(col_width, 3, row_width)
    )
    back_term = lax.dot_general(
        grad_flat, weight_flat, (((1,), (1,)), ((), ())), preferred_element_type=jnp.float32
    )
    both_sums = fold_rows(jnp.stack([projected_term, back_term]))
    projected = both_sums[0]
    back_sum = both_sums[1]
    result = (inputs.astype(jnp.float32) + projected).astype(jnp.bfloat16)
    input_grad = (out_grad.astype(jnp.float32) + back_sum).astype(jnp.bfloat16)
    return (result, input_grad, in_grad, out_w_grad, filter_grad)


def solution(mesh):
    placed = (
        P("row", "col"),
        P("row", "col"),
        P("col", None, "row"),
        P("row", "col"),
        P("row", None),
    )
    return jax.shard_map(
        on_device,
        mesh=mesh,
        in_specs=placed,
        out_specs=(
            P("row", "col"),
            P("row", "col"),
            P("col", None, "row"),
            P("row", "col"),
            P(("row", "col"), None),
        ),
        check_vma=False,
    )
```

```python
import math

import jax
import jax.numpy as jnp
from jax import lax
from jax.experimental import pallas as pl
from jax.experimental.pallas import tpu as pltpu
from jax.sharding import PartitionSpec as P


def rows_in(operand):
    return lax.all_gather(operand, "row", axis=1, tiled=True)


def fold_rows(summand):
    devices = lax.axis_size("row")
    me = lax.axis_index("row")
    lead, rows = summand.shape[0], summand.shape[1] // devices
    parts = summand.astype(jnp.bfloat16).reshape((lead, devices, rows) + summand.shape[2:])
    total = lax.dynamic_index_in_dim(parts, me, 1, keepdims=False).astype(jnp.float32)
    for dist in range(1, devices):
        pairs = [(i, (i + dist) % devices) for i in range(devices)]
        block = lax.dynamic_index_in_dim(parts, (me + dist) % devices, 1, keepdims=False)
        total = total + lax.ppermute(block, "row", pairs).astype(jnp.float32)
    return total


def sum_cols(summand):
    return lax.psum(summand.astype(jnp.bfloat16), "col")


def gate_body(q_ref, k_ref, v_ref, g_ref, t_ref, gated_ref, gq_ref, gk_ref, gv_ref, ts_ref):
    tokens, width = q_ref.shape
    kernel_len = t_ref.shape[0]
    q = q_ref[...].astype(jnp.float32)
    k = k_ref[...].astype(jnp.float32)
    v = v_ref[...].astype(jnp.float32)
    g = g_ref[...].astype(jnp.float32)
    taps = t_ref[...]
    row = lax.broadcasted_iota(jnp.int32, (tokens, width), 0)
    kv = k * v
    kv_lag = [kv]
    for i in range(1, kernel_len):
        kv_lag.append(jnp.where(row >= i, pltpu.roll(kv, i, 0), 0.0))
    conv = taps[0:1, :] * kv_lag[0]
    for i in range(1, kernel_len):
        conv = conv + taps[i : i + 1, :] * kv_lag[i]
    gated_ref[...] = (q * conv).astype(gated_ref.dtype)
    gc = g * q
    gp = taps[0:1, :] * gc
    sums = []
    for i in range(kernel_len):
        if i > 0:
            lead = jnp.where(row < tokens - i, pltpu.roll(gc, tokens - i, 0), 0.0)
            gp = gp + taps[i : i + 1, :] * lead
        sums.append(jnp.sum(gc * kv_lag[i], axis=0, keepdims=True))
    sums.append(jnp.zeros((ts_ref.shape[0] - kernel_len, width), jnp.float32))
    ts_ref[...] = jnp.concatenate(sums, 0)
    gq_ref[...] = (g * conv).astype(gq_ref.dtype)
    gk_ref[...] = (gp * v).astype(gk_ref.dtype)
    gv_ref[...] = (gp * k).astype(gv_ref.dtype)


def gate_kernel(mixed_flat, grad_gated, taps_t, width=128):
    tokens, three_ch = mixed_flat.shape
    channels = three_ch // 3
    kernel_len = taps_t.shape[0]
    tiles = channels // width
    col = lambda off: pl.BlockSpec((tokens, width), lambda j: (0, j + off))
    half = jax.ShapeDtypeStruct((tokens, channels), jnp.bfloat16)
    return pl.pallas_call(
        gate_body,
        grid=(tiles,),
        in_specs=[
            col(0),
            col(tiles),
            col(2 * tiles),
            col(0),
            pl.BlockSpec((kernel_len, width), lambda j: (0, j)),
        ],
        out_specs=[col(0), col(0), col(0), col(0), pl.BlockSpec((8, width), lambda j: (0, j))],
        out_shape=[half, half, half, half, jax.ShapeDtypeStruct((8, channels), jnp.float32)],
        cost_estimate=pl.CostEstimate(
            flops=60 * tokens * channels, transcendentals=0, bytes_accessed=18 * tokens * channels
        ),
    )(mixed_flat, mixed_flat, mixed_flat, grad_gated, taps_t)


def on_device(inputs, out_grad, in_weight, out_weight, filter_taps):
    col_width = inputs.shape[1]
    row_width = out_weight.shape[0]
    weight_flat = in_weight.reshape(col_width, 3 * row_width)
    both_in = rows_in(jnp.stack([inputs, out_grad]))
    whole_in = both_in[0]
    whole_grad = both_in[1]
    all_tokens = whole_in.shape[0]
    grad_scale = 1.0 / math.sqrt(all_tokens)

    in_term = jnp.dot(whole_in, weight_flat, preferred_element_type=jnp.float32)
    dy_term = lax.dot_general(
        whole_grad, out_weight, (((1,), (1,)), ((), ())), preferred_element_type=jnp.float32
    )
    mixed_flat = sum_cols(in_term)
    grad_gated = sum_cols(dy_term)
    gated_all, grad_query, grad_key, grad_value, tap_sums = gate_kernel(
        mixed_flat, grad_gated, filter_taps.T
    )

    projected_term = jnp.dot(gated_all, out_weight, preferred_element_type=jnp.float32)
    out_w_grad = (
        lax.dot_general(
            gated_all, whole_grad, (((0,), (0,)), ((), ())), preferred_element_type=jnp.float32
        )
        * grad_scale
    ).astype(jnp.bfloat16)
    cols = lax.axis_size("col")
    own = row_width // cols
    kernel_len = filter_taps.shape[1]
    filter_grad = (
        lax.dynamic_slice_in_dim(tap_sums[:kernel_len], lax.axis_index("col") * own, own, 1).T
        * grad_scale
    )
    grad_flat = jnp.concatenate([grad_query, grad_key, grad_value], axis=1)
    in_grad = (
        (
            lax.dot_general(
                whole_in, grad_flat, (((0,), (0,)), ((), ())), preferred_element_type=jnp.float32
            )
            * grad_scale
        )
        .astype(jnp.bfloat16)
        .reshape(col_width, 3, row_width)
    )
    back_term = lax.dot_general(
        grad_flat, weight_flat, (((1,), (1,)), ((), ())), preferred_element_type=jnp.float32
    )
    both_sums = fold_rows(jnp.stack([projected_term, back_term]))
    projected = both_sums[0]
    back_sum = both_sums[1]
    result = (inputs.astype(jnp.float32) + projected).astype(jnp.bfloat16)
    input_grad = (out_grad.astype(jnp.float32) + back_sum).astype(jnp.bfloat16)
    return (result, input_grad, in_grad, out_w_grad, filter_grad)


def solution(mesh):
    placed = (
        P("row", "col"),
        P("row", "col"),
        P("col", None, "row"),
        P("row", "col"),
        P("row", None),
    )
    return jax.shard_map(
        on_device,
        mesh=mesh,
        in_specs=placed,
        out_specs=(
            P("row", "col"),
            P("row", "col"),
            P("col", None, "row"),
            P("row", "col"),
            P(("row", "col"), None),
        ),
        check_vma=False,
    )
```
